128 devices in a mesh: group: 4 (over y), local: 32 (over x, z, core).
Axes of the slice: x: 4, y: 4, z: 4, core: 2. Of those that a mesh axis runs over, the one named last changes fastest.
Arguments:
- tokens: bfloat16 [16384, 3584], P(('group', 'local')), may hold values from -6 to 6
- grad_out: bfloat16 [16384, 3584], P(('group', 'local')), may hold values from -6 to 6
- expert_ids: int32 [16384, 4], P(('group', 'local')), may hold values from 0 to 127, as said below
- combine: bfloat16 [16384, 4], P(('group', 'local')), may hold values from 0.099609375 to 1
- gate_weight: bfloat16 [128, 3584, 1024], P(('group', 'local')), may hold values from -0.09375 to 0.09375
- up_weight: bfloat16 [128, 3584, 1024], P(('group', 'local')), may hold values from -0.09375 to 0.09375
- down_weight: bfloat16 [128, 1024, 3584], P(('group', 'local')), may hold values from -0.1875 to 0.1875
Outputs:
- grad_tokens: bfloat16 [16384, 3584], P(('group', 'local'))
- grad_combine: bfloat16 [16384, 4], P(('group', 'local'))
The draws below stay inside these ranges and needn't reach their ends.
Inputs may be any that keep to these rules, and one draw needn't show every extreme that they name: `expert_ids`: each token names 4 different experts; expert e lies in node group e // 32. The first 2 experts of a token lie in one group and the other 2 in another, so a token uses 2 groups. The tokens of each device choose every group exactly 128//2 times. The tokens of one device name one expert at most 6 times, and in every draw some expert is named 6 times by the tokens of every device.
All inputs are finite; a program needn't handle non-finite values.
Results may differ from the reference program's by a relative error of at most 0.0058.
Values may be sent and summed in bfloat16 or wider, within the bound.
No kernel may reach another device: no remote copies, remote signals or barrier semaphores. Data moves between devices by JAX's collectives and lax.ppermute only.
A program may use at most 128 MiB of HBM per device.

```python
import math
import jax
import jax.numpy as jnp
from jax import lax

D = 3584
FF = 1024
TOP = 4
TOK_DEV = 128
EXPERTS = 128
TOKENS = 16384
MEAN_PAIR = 4
PAIR_CAP = 6
N_GROUP = 4
N_LOCAL = 32


def draw_expert_ids(key, part):
    key_roles = jax.random.fold_in(key, 11)
    key_perm = jax.random.fold_in(key, 12)
    key_hot = jax.random.fold_in(key, 13)
    devices = N_GROUP * N_LOCAL
    roles = jax.vmap(lambda single: jax.random.permutation(single, TOK_DEV))(jax.random.split(key_roles, devices)).astype(jnp.int32)
    quarter = TOK_DEV // 4
    first = roles % 4
    within = roles // 4
    offset = jnp.where(within < 3 * quarter // 8, 1, jnp.where(within < 6 * quarter // 8, 3, 2))
    second = (first + offset) % 4
    rounds = MEAN_PAIR
    hot_rounds = (rounds + 1) // 2
    perms = jax.vmap(lambda single: jax.random.permutation(single, N_LOCAL))(jax.random.split(key_perm, devices * 4 * rounds))
    perms = perms.astype(jnp.int32).reshape(devices, 4, rounds, N_LOCAL)
    hottest = jax.random.randint(key_hot, (4,), 0, N_LOCAL).astype(jnp.int32)
    hot_block = hottest[None, :, None, None]
    position = jnp.argmax(perms == hot_block, axis=3).astype(jnp.int32)
    target = (position + 2) % N_LOCAL
    column = jnp.arange(N_LOCAL, dtype=jnp.int32)[None, None, None, :]
    round_index = jnp.arange(rounds, dtype=jnp.int32)[None, None, :, None]
    replace = (column == target[..., None]) & (round_index < hot_rounds)
    perms = jnp.where(replace, hot_block, perms)
    pool_flat = perms.reshape(devices, 4 * TOK_DEV)

    def choose(group, rank_in, shift):
        index = group * TOK_DEV + 2 * rank_in + shift
        return group * N_LOCAL + jnp.take_along_axis(pool_flat, index, axis=1)
    expert_zero = choose(first, within, 0)
    expert_one = choose(first, within, 1)
    expert_two = choose(second, quarter + within, 0)
    expert_three = choose(second, quarter + within, 1)
    stacked = jnp.stack([expert_zero, expert_one, expert_two, expert_three], axis=-1)
    return stacked.reshape(devices * TOK_DEV, 4).astype(jnp.int32)


def steps_of(stream_key, extent, shards, least, high):
    def one(axis_at, shards_of):
        heights = jax.random.uniform(jax.random.fold_in(jax.random.fold_in(stream_key, 6), axis_at), (shards_of,), jnp.float32, least / len(shards), high / len(shards))
        return jnp.repeat(jnp.exp(heights), extent[axis_at] // shards_of).reshape((-1,) + (1,) * (len(extent) - axis_at - 1))

    factor_of = one(*shards[0])
    for cut in shards[1:]:
        factor_of = factor_of * one(*cut)
    return factor_of


def noise(stream_key, dims, scale, most, shards=(), kind=jnp.bfloat16):
    array = scale * jax.random.normal(stream_key, dims, jnp.float32)
    if shards:
        array = array * steps_of(stream_key, dims, shards, -0.22, 0.18)
    return jnp.clip(array, -most, most).astype(kind)


def setup_inputs(seed: int = 0) -> dict:
    splits = jax.random.split(jax.random.key(seed), 8)
    tokens = noise(splits[0], (TOKENS, D), 1.0, 6.0, ((0, 128),))
    grad_out = noise(splits[1], (TOKENS, D), 1.0, 6.0, ((0, 128),))
    expert_ids = draw_expert_ids(jax.random.fold_in(splits[7], 71), 0)
    combine = jnp.clip(jnp.exp(math.log(1.0) - 2.306499 * jax.random.uniform(splits[3], (TOKENS, TOP), jnp.float32) ** steps_of(splits[3], (TOKENS, TOP), ((0, 128),), -0.2, 0.2)), 0.099609375, 1.0).astype(jnp.bfloat16)
    gate_weight = noise(splits[4], (EXPERTS, D, FF), D ** -0.5, 0.09375, ((0, 128),))
    up_weight = noise(splits[5], (EXPERTS, D, FF), D ** -0.5, 0.09375, ((0, 128),))
    down_weight = noise(splits[6], (EXPERTS, FF, D), FF ** -0.5, 0.1875, ((0, 128),))
    return {"tokens": tokens, "grad_out": grad_out, "expert_ids": expert_ids, "combine": combine, "gate_weight": gate_weight, "up_weight": up_weight, "down_weight": down_weight}


def expert_rows(rows_x, rows_dy, rows_p, gate_mat, up_mat, down_mat):
    gate_pre = jnp.dot(rows_x, gate_mat, preferred_element_type=jnp.float32)
    up_pre = jnp.dot(rows_x, up_mat, preferred_element_type=jnp.float32)
    sigmoid_gate = jax.nn.sigmoid(gate_pre)
    active = gate_pre * sigmoid_gate
    hidden = (active * up_pre).astype(jnp.bfloat16)
    output = jnp.dot(hidden, down_mat, preferred_element_type=jnp.float32)
    grad_weight = jnp.sum(rows_dy.astype(jnp.float32) * output, axis=1).astype(jnp.bfloat16)
    back_hidden = lax.dot_general(rows_dy, down_mat, (((1,), (1,)), ((), ())), preferred_element_type=jnp.float32)
    back_hidden = back_hidden * rows_p.astype(jnp.float32)[:, None]
    grad_gate = (back_hidden * up_pre * sigmoid_gate * (1.0 + gate_pre * (1.0 - sigmoid_gate))).astype(jnp.bfloat16)
    grad_up = (back_hidden * active).astype(jnp.bfloat16)
    contrib = lax.dot_general(grad_gate, gate_mat, (((1,), (1,)), ((), ())), preferred_element_type=jnp.float32)
    contrib = contrib + lax.dot_general(grad_up, up_mat, (((1,), (1,)), ((), ())), preferred_element_type=jnp.float32)
    return contrib.astype(jnp.bfloat16), grad_weight


def reference(tokens, grad_out, expert_ids, combine, gate_weight, up_weight, down_weight):
    flat_ids = expert_ids.reshape(-1).astype(jnp.int32)
    assign_count = flat_ids.shape[0]
    by_expert = jnp.argsort(flat_ids, stable=True).astype(jnp.int32)
    counts = jax.ops.segment_sum(jnp.ones((assign_count,), jnp.int32), flat_ids, num_segments=EXPERTS).astype(jnp.int32)
    starts = (jnp.cumsum(counts) - counts).astype(jnp.int32)
    capacity = EXPERTS * PAIR_CAP
    padded_order = jnp.concatenate([by_expert, jnp.zeros((capacity,), jnp.int32)])
    flat_weight = combine.reshape(-1)
    positions = jnp.arange(capacity, dtype=jnp.int32)

    def visit(state_pair, inputs):
        totals, weight_grads = state_pair
        expert, gate_mat, up_mat, down_mat = inputs
        picked = lax.dynamic_slice(padded_order, (starts[expert],), (capacity,))
        usable = positions < counts[expert]
        token_index = picked // TOP
        rows_x = jnp.where(usable[:, None], tokens[token_index], jnp.zeros((), tokens.dtype))
        rows_dy = jnp.where(usable[:, None], grad_out[token_index], jnp.zeros((), grad_out.dtype))
        rows_p = jnp.where(usable, flat_weight[picked], jnp.zeros((), combine.dtype))
        contrib, grad_weight = expert_rows(rows_x, rows_dy, rows_p, gate_mat, up_mat, down_mat)
        totals = totals.at[token_index].add(jnp.where(usable[:, None], contrib.astype(jnp.float32), 0.0))
        weight_grads = weight_grads.at[picked].add(jnp.where(usable, grad_weight.astype(jnp.float32), 0.0))
        return (totals, weight_grads), None

    initial = (jnp.zeros((TOKENS, D), jnp.float32), jnp.zeros((assign_count,), jnp.float32))
    final_state, _ = lax.scan(visit, initial, (jnp.arange(EXPERTS, dtype=jnp.int32), gate_weight, up_weight, down_weight))
    totals, weight_grads = final_state
    return totals.astype(jnp.bfloat16), weight_grads.reshape(TOKENS, TOP).astype(jnp.bfloat16)
```

```python
import jax
import jax.numpy as jnp
from jax import lax
from jax.sharding import PartitionSpec as P


def _t_dot(a, b):
    return lax.dot_general(a, b, (((1,), (1,)), ((), ())), preferred_element_type=jnp.float32)


def local(tokens, grad_out, expert_ids, combine, gate_weight, up_weight, down_weight):
    token_rows, model_width = tokens.shape
    top_count = expert_ids.shape[1]
    group_count = lax.axis_size("group")
    local_count = lax.axis_size("local")
    expert_count = group_count * local_count
    mean_pair = token_rows * top_count // expert_count
    pair_cap = mean_pair + (mean_pair + 1) // 2
    slot_cap = (pair_cap + 7) // 8 * 8
    gate_mat = gate_weight[0]
    up_mat = up_weight[0]
    down_mat = down_weight[0]
    ff = gate_mat.shape[1]
    assign_count = token_rows * top_count
    lane = 128
    targets = expert_ids.reshape(assign_count)
    one_hot = (targets[:, None] == jnp.arange(expert_count, dtype=jnp.int32)[None, :]).astype(
        jnp.int32
    )
    rank_in = jnp.sum((jnp.cumsum(one_hot, axis=0) - 1) * one_hot, axis=1)
    slot_of = targets * slot_cap + rank_in
    slot_total = expert_count * slot_cap
    sel = slot_of[None, :] == jnp.arange(slot_total, dtype=jnp.int32)[:, None]
    sel_a = sel.astype(jnp.bfloat16)
    sel_t = jnp.any(sel.reshape(slot_total, token_rows, top_count), axis=2).astype(jnp.bfloat16)

    send_x = jnp.dot(sel_t, tokens, preferred_element_type=jnp.bfloat16)
    p_block = jnp.zeros((assign_count, lane), jnp.bfloat16).at[:, 0].set(combine.reshape(assign_count))
    dy_rep = jnp.broadcast_to(grad_out[:, None, :], (token_rows, top_count, model_width)).reshape(
        assign_count, model_width
    )
    send_dyp = jnp.dot(
        sel_a, jnp.concatenate([dy_rep, p_block], axis=1), preferred_element_type=jnp.bfloat16
    )

    def a2a(v):
        v = v.reshape(expert_count, slot_cap, v.shape[-1])
        v = lax.all_to_all(v, ("group", "local"), split_axis=0, concat_axis=0, tiled=True)
        return v.reshape(slot_total, v.shape[-1])

    rows_x = a2a(send_x)
    gate_pre = jnp.dot(rows_x, gate_mat, preferred_element_type=jnp.float32)
    up_pre = jnp.dot(rows_x, up_mat, preferred_element_type=jnp.float32)
    sigmoid_gate = jax.nn.sigmoid(gate_pre)
    active = gate_pre * sigmoid_gate
    hidden = (active * up_pre).astype(jnp.bfloat16)
    output = jnp.dot(hidden, down_mat, preferred_element_type=jnp.float32)

    rows_dyp = a2a(send_dyp)
    rows_dy = rows_dyp[:, :model_width]
    rows_p = rows_dyp[:, model_width]
    grad_weight = jnp.sum(rows_dy.astype(jnp.float32) * output, axis=1).astype(jnp.bfloat16)
    back_hidden = _t_dot(rows_dy, down_mat)
    back_hidden = back_hidden * rows_p.astype(jnp.float32)[:, None]
    grad_gate = (
        back_hidden * up_pre * sigmoid_gate * (1.0 + gate_pre * (1.0 - sigmoid_gate))
    ).astype(jnp.bfloat16)
    grad_up = (back_hidden * active).astype(jnp.bfloat16)

    half = model_width // 2
    contrib_a = (_t_dot(grad_gate, gate_mat[:half]) + _t_dot(grad_up, up_mat[:half])).astype(
        jnp.bfloat16
    )
    gw_block = jnp.zeros((slot_total, lane), jnp.bfloat16).at[:, 0].set(grad_weight)
    back_a = a2a(jnp.concatenate([contrib_a, gw_block], axis=1))
    contrib_b = (_t_dot(grad_gate, gate_mat[half:]) + _t_dot(grad_up, up_mat[half:])).astype(
        jnp.bfloat16
    )
    back_b = a2a(contrib_b)

    sum_a = jnp.dot(sel_t.T, back_a[:, :half], preferred_element_type=jnp.float32)
    sum_b = jnp.dot(sel_t.T, back_b, preferred_element_type=jnp.float32)
    grad_tokens = jnp.concatenate([sum_a, sum_b], axis=1).astype(jnp.bfloat16)
    gw_back = jnp.dot(sel_a.T, back_a[:, half:], preferred_element_type=jnp.float32)
    grad_combine = gw_back[:, 0].astype(jnp.bfloat16).reshape(token_rows, top_count)
    return (grad_tokens, grad_combine)


def solution(mesh):
    placed = (
        P(("group", "local"), None),
        P(("group", "local"), None),
        P(("group", "local"), None),
        P(("group", "local"), None),
        P(("group", "local"), None, None),
        P(("group", "local"), None, None),
        P(("group", "local"), None, None),
    )
    return jax.shard_map(
        local,
        mesh=mesh,
        in_specs=placed,
        out_specs=(P(("group", "local"), None), P(("group", "local"), None)),
        check_vma=False,
    )
```

```python
import jax
import jax.numpy as jnp
from jax import lax
from jax.sharding import PartitionSpec as P


def _t_dot(a, b):
    return lax.dot_general(a, b, (((1,), (1,)), ((), ())), preferred_element_type=jnp.float32)


def _rank(keys, count):
    hot = (keys[:, None] == jnp.arange(count, dtype=jnp.int32)[None, :]).astype(jnp.int32)
    return jnp.sum((jnp.cumsum(hot, axis=0) - 1) * hot, axis=1)


def _pick(slots, total):
    return slots[None, :] == jnp.arange(total, dtype=jnp.int32)[:, None]


def local(tokens, grad_out, expert_ids, combine, gate_weight, up_weight, down_weight):
    token_rows, model_width = tokens.shape
    top_count = expert_ids.shape[1]
    group_count = lax.axis_size("group")
    local_count = lax.axis_size("local")
    expert_count = group_count * local_count
    mean_pair = token_rows * top_count // expert_count
    pair_cap = mean_pair + (mean_pair + 1) // 2
    per_half = top_count // 2
    n_pairs = token_rows * 2
    per_group = n_pairs // group_count
    cap2 = group_count * pair_cap
    slots2 = local_count * cap2
    lane = 128
    blk = (local_count + per_half + lane - 1) // lane * lane
    wide = 2 * model_width
    gate_mat = gate_weight[0]
    up_mat = up_weight[0]
    down_mat = down_weight[0]
    l_me = lax.axis_index("local")
    bf = jnp.bfloat16

    halves = expert_ids.reshape(n_pairs, per_half)
    pair_group = halves[:, 0] // local_count
    pair_loc = halves % local_count
    pair_comb = combine.reshape(n_pairs, per_half)
    slot1 = pair_group * per_group + _rank(pair_group, group_count)
    sel1 = _pick(slot1, n_pairs).astype(bf)
    cols = jnp.arange(blk, dtype=jnp.int32)
    cvec = jnp.sum(
        jnp.where(pair_loc[:, :, None] == cols[None, None, :], pair_comb[:, :, None], 0.0), axis=1
    )
    for j in range(per_half):
        cvec = jnp.where(cols[None, :] == local_count + j, pair_loc[:, j : j + 1].astype(jnp.float32), cvec)
    rep = lambda v: jnp.broadcast_to(v[:, None, :], (token_rows, 2, v.shape[-1])).reshape(n_pairs, -1)
    payload1 = jnp.concatenate([rep(tokens), rep(grad_out), cvec.astype(bf)], axis=1)
    send1 = jnp.dot(sel1, payload1, preferred_element_type=bf)
    recv1 = lax.all_to_all(
        send1.reshape(group_count, per_group, -1), "group", 0, 0, tiled=True
    ).reshape(n_pairs, -1)

    loc_q = recv1[:, wide + local_count : wide + local_count + per_half].astype(jnp.int32).reshape(-1)
    slot2 = loc_q * cap2 + _rank(loc_q, local_count)
    sel2_q = _pick(slot2, slots2)
    sel2 = jnp.any(sel2_q.reshape(slots2, n_pairs, per_half), axis=2).astype(bf)

    def a2a_local(v):
        v = v.reshape(local_count, cap2, v.shape[-1])
        v = lax.all_to_all(v, "local", 0, 0, tiled=True)
        return v.reshape(slots2, v.shape[-1])

    rows_x = a2a_local(jnp.dot(sel2, recv1[:, :model_width], preferred_element_type=bf))
    rows_dyp = a2a_local(jnp.dot(sel2, recv1[:, model_width:], preferred_element_type=bf))

    gate_pre = jnp.dot(rows_x, gate_mat, preferred_element_type=jnp.float32)
    up_pre = jnp.dot(rows_x, up_mat, preferred_element_type=jnp.float32)
    sigmoid_gate = jax.nn.sigmoid(gate_pre)
    active = gate_pre * sigmoid_gate
    hidden = (active * up_pre).astype(bf)
    output = jnp.dot(hidden, down_mat, preferred_element_type=jnp.float32)
    rows_dy = rows_dyp[:, :model_width]
    mine = (cols == l_me).astype(jnp.float32)
    rows_p = jnp.sum(rows_dyp[:, model_width:].astype(jnp.float32) * mine[None, :], axis=1)
    grad_weight = jnp.sum(rows_dy.astype(jnp.float32) * output, axis=1).astype(bf)
    back_hidden = _t_dot(rows_dy, down_mat)
    back_hidden = back_hidden * rows_p[:, None]
    grad_gate = (
        back_hidden * up_pre * sigmoid_gate * (1.0 + gate_pre * (1.0 - sigmoid_gate))
    ).astype(bf)
    grad_up = (back_hidden * active).astype(bf)

    half = model_width // 2
    contrib_a = (_t_dot(grad_gate, gate_mat[:half]) + _t_dot(grad_up, up_mat[:half])).astype(bf)
    gw_block = jnp.zeros((slots2, lane), bf).at[:, 0].set(grad_weight)
    back_a = a2a_local(jnp.concatenate([contrib_a, gw_block], axis=1))
    contrib_b = (_t_dot(grad_gate, gate_mat[half:]) + _t_dot(grad_up, up_mat[half:])).astype(bf)
    back_b = a2a_local(contrib_b)

    sum_a = jnp.dot(sel2.T, back_a[:, :half], preferred_element_type=jnp.float32)
    sum_b = jnp.dot(sel2.T, back_b, preferred_element_type=jnp.float32)
    gw_q = jnp.dot(sel2_q.astype(bf).T, back_a[:, half:], preferred_element_type=jnp.float32)
    gw_pair = gw_q[:, 0].reshape(n_pairs, per_half)
    gw_blk = jnp.zeros((n_pairs, lane), jnp.float32).at[:, :per_half].set(gw_pair)
    back1 = jnp.concatenate([sum_a, sum_b, gw_blk], axis=1).astype(bf)
    recv_b1 = lax.all_to_all(
        back1.reshape(group_count, per_group, -1), "group", 0, 0, tiled=True
    ).reshape(n_pairs, -1)

    sel1_t = jnp.any(
        sel1.astype(jnp.bool_).reshape(n_pairs, token_rows, 2), axis=2
    ).astype(bf)
    grad_tokens = jnp.dot(
        sel1_t.T, recv_b1[:, :model_width], preferred_element_type=jnp.float32
    ).astype(bf)
    gw_back = jnp.dot(sel1.T, recv_b1[:, model_width:], preferred_element_type=jnp.float32)
    grad_combine = gw_back[:, :per_half].astype(bf).reshape(token_rows, top_count)
    return (grad_tokens, grad_combine)


def solution(mesh):
    placed = (
        P(("group", "local"), None),
        P(("group", "local"), None),
        P(("group", "local"), None),
        P(("group", "local"), None),
        P(("group", "local"), None, None),
        P(("group", "local"), None, None),
        P(("group", "local"), None, None),
    )
    return jax.shard_map(
        local,
        mesh=mesh,
        in_specs=placed,
        out_specs=(P(("group", "local"), None), P(("group", "local"), None)),
        check_vma=False,
    )
```

```python
import jax
import jax.numpy as jnp
from jax import lax
from jax.sharding import PartitionSpec as P


def _t_dot(a, b):
    return lax.dot_general(a, b, (((1,), (1,)), ((), ())), preferred_element_type=jnp.float32)


def local(tokens, grad_out, expert_ids, combine, gate_weight, up_weight, down_weight):
    token_rows, model_width = tokens.shape
    top_count = expert_ids.shape[1]
    group_count = lax.axis_size("group")
    local_count = lax.axis_size("local")
    expert_count = group_count * local_count
    mean_pair = token_rows * top_count // expert_count
    pair_cap = mean_pair + (mean_pair + 1) // 2
    slot_cap = pair_cap
    gate_mat = gate_weight[0]
    up_mat = up_weight[0]
    down_mat = down_weight[0]
    ff = gate_mat.shape[1]
    assign_count = token_rows * top_count
    lane = 128
    targets = expert_ids.reshape(assign_count)
    one_hot = (targets[:, None] == jnp.arange(expert_count, dtype=jnp.int32)[None, :]).astype(
        jnp.int32
    )
    rank_in = jnp.sum((jnp.cumsum(one_hot, axis=0) - 1) * one_hot, axis=1)
    slot_of = targets * slot_cap + rank_in
    slot_total = expert_count * slot_cap
    sel = slot_of[None, :] == jnp.arange(slot_total, dtype=jnp.int32)[:, None]
    sel_a = sel.astype(jnp.bfloat16)
    sel_t = jnp.any(sel.reshape(slot_total, token_rows, top_count), axis=2).astype(jnp.bfloat16)

    send_x = jnp.dot(sel_t, tokens, preferred_element_type=jnp.bfloat16)
    p_block = jnp.zeros((assign_count, lane), jnp.bfloat16).at[:, 0].set(combine.reshape(assign_count))
    dy_rep = jnp.broadcast_to(grad_out[:, None, :], (token_rows, top_count, model_width)).reshape(
        assign_count, model_width
    )
    send_dyp = jnp.dot(
        sel_a, jnp.concatenate([dy_rep, p_block], axis=1), preferred_element_type=jnp.bfloat16
    )

    def a2a(v):
        width = v.shape[-1]
        v = v.reshape(expert_count, slot_cap * width // lane, lane)
        v = lax.all_to_all(v, ("group", "local"), split_axis=0, concat_axis=0, tiled=True)
        return v.reshape(slot_total, width)

    rows_x = a2a(send_x)
    gate_pre = jnp.dot(rows_x, gate_mat, preferred_element_type=jnp.float32)
    up_pre = jnp.dot(rows_x, up_mat, preferred_element_type=jnp.float32)
    sigmoid_gate = jax.nn.sigmoid(gate_pre)
    active = gate_pre * sigmoid_gate
    hidden = (active * up_pre).astype(jnp.bfloat16)
    output = jnp.dot(hidden, down_mat, preferred_element_type=jnp.float32)

    rows_dyp = a2a(send_dyp)
    rows_dy = rows_dyp[:, :model_width]
    rows_p = rows_dyp[:, model_width]
    grad_weight = jnp.sum(rows_dy.astype(jnp.float32) * output, axis=1).astype(jnp.bfloat16)
    back_hidden = _t_dot(rows_dy, down_mat)
    back_hidden = back_hidden * rows_p.astype(jnp.float32)[:, None]
    grad_gate = (
        back_hidden * up_pre * sigmoid_gate * (1.0 + gate_pre * (1.0 - sigmoid_gate))
    ).astype(jnp.bfloat16)
    grad_up = (back_hidden * active).astype(jnp.bfloat16)

    half = model_width // 2
    contrib_a = (_t_dot(grad_gate, gate_mat[:half]) + _t_dot(grad_up, up_mat[:half])).astype(
        jnp.bfloat16
    )
    gw_block = jnp.zeros((slot_total, lane), jnp.bfloat16).at[:, 0].set(grad_weight)
    back_a = a2a(jnp.concatenate([contrib_a, gw_block], axis=1))
    contrib_b = (_t_dot(grad_gate, gate_mat[half:]) + _t_dot(grad_up, up_mat[half:])).astype(
        jnp.bfloat16
    )
    back_b = a2a(contrib_b)

    sum_a = jnp.dot(sel_t.T, back_a[:, :half], preferred_element_type=jnp.float32)
    sum_b = jnp.dot(sel_t.T, back_b, preferred_element_type=jnp.float32)
    grad_tokens = jnp.concatenate([sum_a, sum_b], axis=1).astype(jnp.bfloat16)
    gw_back = jnp.dot(sel_a.T, back_a[:, half:], preferred_element_type=jnp.float32)
    grad_combine = gw_back[:, 0].astype(jnp.bfloat16).reshape(token_rows, top_count)
    return (grad_tokens, grad_combine)


def solution(mesh):
    placed = (
        P(("group", "local"), None),
        P(("group", "local"), None),
        P(("group", "local"), None),
        P(("group", "local"), None),
        P(("group", "local"), None, None),
        P(("group", "local"), None, None),
        P(("group", "local"), None, None),
    )
    return jax.shard_map(
        local,
        mesh=mesh,
        in_specs=placed,
        out_specs=(P(("group", "local"), None), P(("group", "local"), None)),
        check_vma=False,
    )
```

```python
import jax
import jax.numpy as jnp
from jax import lax
from jax.sharding import PartitionSpec as P


def _t_dot(a, b):
    return lax.dot_general(a, b, (((1,), (1,)), ((), ())), preferred_element_type=jnp.float32)


def expert_rows(rows, model_width, lane, gate_mat, up_mat, down_mat):
    rows_x = rows[:, :model_width]
    rows_dy = rows[:, model_width : 2 * model_width]
    rows_p = rows[:, 2 * model_width]
    gate_pre = jnp.dot(rows_x, gate_mat, preferred_element_type=jnp.float32)
    up_pre = jnp.dot(rows_x, up_mat, preferred_element_type=jnp.float32)
    sigmoid_gate = jax.nn.sigmoid(gate_pre)
    active = gate_pre * sigmoid_gate
    hidden = (active * up_pre).astype(jnp.bfloat16)
    output = jnp.dot(hidden, down_mat, preferred_element_type=jnp.float32)
    grad_weight = jnp.sum(rows_dy.astype(jnp.float32) * output, axis=1).astype(jnp.bfloat16)
    back_hidden = _t_dot(rows_dy, down_mat)
    back_hidden = back_hidden * rows_p.astype(jnp.float32)[:, None]
    grad_gate = (
        back_hidden * up_pre * sigmoid_gate * (1.0 + gate_pre * (1.0 - sigmoid_gate))
    ).astype(jnp.bfloat16)
    grad_up = (back_hidden * active).astype(jnp.bfloat16)
    contrib = (_t_dot(grad_gate, gate_mat) + _t_dot(grad_up, up_mat)).astype(jnp.bfloat16)
    gw_block = jnp.zeros((rows.shape[0], lane), jnp.bfloat16).at[:, 0].set(grad_weight)
    return jnp.concatenate([contrib, gw_block], axis=1)


def local(tokens, grad_out, expert_ids, combine, gate_weight, up_weight, down_weight):
    token_rows, model_width = tokens.shape
    top_count = expert_ids.shape[1]
    group_count = lax.axis_size("group")
    local_count = lax.axis_size("local")
    expert_count = group_count * local_count
    mean_pair = token_rows * top_count // expert_count
    pair_cap = mean_pair + (mean_pair + 1) // 2
    n_chunks = 2
    chunk_cap = (pair_cap + n_chunks - 1) // n_chunks
    chunk_slots = expert_count * chunk_cap
    gate_mat = gate_weight[0]
    up_mat = up_weight[0]
    down_mat = down_weight[0]
    assign_count = token_rows * top_count
    lane = 128
    targets = expert_ids.reshape(assign_count)
    one_hot = (targets[:, None] == jnp.arange(expert_count, dtype=jnp.int32)[None, :]).astype(
        jnp.int32
    )
    rank_in = jnp.sum((jnp.cumsum(one_hot, axis=0) - 1) * one_hot, axis=1)
    slot_of = (
        (rank_in // chunk_cap) * chunk_slots + targets * chunk_cap + rank_in % chunk_cap
    )
    p_block = jnp.zeros((assign_count, lane), jnp.bfloat16).at[:, 0].set(
        combine.reshape(assign_count)
    )
    rep = lambda v: jnp.broadcast_to(
        v[:, None, :], (token_rows, top_count, model_width)
    ).reshape(assign_count, model_width)
    payload = jnp.concatenate([rep(tokens), rep(grad_out), p_block], axis=1)

    def a2a(v):
        width = v.shape[-1]
        v = v.reshape(expert_count, chunk_cap * width // lane, lane)
        v = lax.all_to_all(v, ("group", "local"), split_axis=0, concat_axis=0, tiled=True)
        return v.reshape(chunk_slots, width)

    grad_sum = None
    gw_sum = None
    for c in range(n_chunks):
        sel = slot_of[None, :] == (c * chunk_slots + jnp.arange(chunk_slots, dtype=jnp.int32))[:, None]
        sel_a = sel.astype(jnp.bfloat16)
        rows = a2a(jnp.dot(sel_a, payload, preferred_element_type=jnp.bfloat16))
        back = a2a(expert_rows(rows, model_width, lane, gate_mat, up_mat, down_mat))
        sel_t = jnp.any(sel.reshape(chunk_slots, token_rows, top_count), axis=2).astype(
            jnp.bfloat16
        )
        part = jnp.dot(sel_t.T, back[:, :model_width], preferred_element_type=jnp.float32)
        gw_part = jnp.dot(sel_a.T, back[:, model_width:], preferred_element_type=jnp.float32)
        grad_sum = part if grad_sum is None else grad_sum + part
        gw_sum = gw_part if gw_sum is None else gw_sum + gw_part
    grad_tokens = grad_sum.astype(jnp.bfloat16)
    grad_combine = gw_sum[:, 0].astype(jnp.bfloat16).reshape(token_rows, top_count)
    return (grad_tokens, grad_combine)


def solution(mesh):
    placed = (
        P(("group", "local"), None),
        P(("group", "local"), None),
        P(("group", "local"), None),
        P(("group", "local"), None),
        P(("group", "local"), None, None),
        P(("group", "local"), None, None),
        P(("group", "local"), None, None),
    )
    return jax.shard_map(
        local,
        mesh=mesh,
        in_specs=placed,
        out_specs=(P(("group", "local"), None), P(("group", "local"), None)),
        check_vma=False,
    )
```

```python
import jax
import jax.numpy as jnp
from jax import lax
from jax.sharding import PartitionSpec as P


def _t_dot(a, b):
    return lax.dot_general(a, b, (((1,), (1,)), ((), ())), preferred_element_type=jnp.float32)


def local(tokens, grad_out, expert_ids, combine, gate_weight, up_weight, down_weight):
    token_rows, model_width = tokens.shape
    top_count = expert_ids.shape[1]
    group_count = lax.axis_size("group")
    local_count = lax.axis_size("local")
    expert_count = group_count * local_count
    mean_pair = token_rows * top_count // expert_count
    pair_cap = mean_pair + (mean_pair + 1) // 2
    slot_cap = pair_cap
    gate_mat = gate_weight[0]
    up_mat = up_weight[0]
    down_mat = down_weight[0]
    ff = gate_mat.shape[1]
    assign_count = token_rows * top_count
    lane = 128
    targets = expert_ids.reshape(assign_count)
    one_hot = (targets[:, None] == jnp.arange(expert_count, dtype=jnp.int32)[None, :]).astype(
        jnp.int32
    )
    rank_in = jnp.sum((jnp.cumsum(one_hot, axis=0) - 1) * one_hot, axis=1)
    slot_of = targets * slot_cap + rank_in
    slot_total = expert_count * slot_cap
    sel = slot_of[None, :] == jnp.arange(slot_total, dtype=jnp.int32)[:, None]
    sel_a = sel.astype(jnp.bfloat16)
    sel_t = jnp.any(sel.reshape(slot_total, token_rows, top_count), axis=2).astype(jnp.bfloat16)

    send_x = jnp.dot(sel_t, tokens, preferred_element_type=jnp.bfloat16)
    p_block = jnp.zeros((assign_count, lane), jnp.bfloat16).at[:, 0].set(combine.reshape(assign_count))
    dy_rep = jnp.broadcast_to(grad_out[:, None, :], (token_rows, top_count, model_width)).reshape(
        assign_count, model_width
    )
    send_dyp = jnp.dot(
        sel_a, jnp.concatenate([dy_rep, p_block], axis=1), preferred_element_type=jnp.bfloat16
    )

    def a2a(v):
        width = v.shape[-1]
        v = v.reshape(expert_count, slot_cap * width // lane, lane)
        v = lax.all_to_all(v, ("group", "local"), split_axis=0, concat_axis=0, tiled=True)
        return v.reshape(slot_total, width)

    rows_x = a2a(send_x)
    gate_pre = jnp.dot(rows_x, gate_mat, preferred_element_type=jnp.float32)
    up_pre = jnp.dot(rows_x, up_mat, preferred_element_type=jnp.float32)
    sigmoid_gate = jax.nn.sigmoid(gate_pre)
    active = gate_pre * sigmoid_gate
    hidden = (active * up_pre).astype(jnp.bfloat16)
    output = jnp.dot(hidden, down_mat, preferred_element_type=jnp.float32)

    rows_dyp = a2a(send_dyp)
    rows_dy = rows_dyp[:, :model_width]
    rows_p = rows_dyp[:, model_width]
    grad_weight = jnp.sum(rows_dy.astype(jnp.float32) * output, axis=1).astype(jnp.bfloat16)
    back_hidden = _t_dot(rows_dy, down_mat)
    back_hidden = back_hidden * rows_p.astype(jnp.float32)[:, None]
    grad_gate = (
        back_hidden * up_pre * sigmoid_gate * (1.0 + gate_pre * (1.0 - sigmoid_gate))
    ).astype(jnp.bfloat16)
    grad_up = (back_hidden * active).astype(jnp.bfloat16)

    half = model_width // 4
    contrib_a = (_t_dot(grad_gate, gate_mat[:half]) + _t_dot(grad_up, up_mat[:half])).astype(
        jnp.bfloat16
    )
    gw_block = jnp.zeros((slot_total, lane), jnp.bfloat16).at[:, 0].set(grad_weight)
    back_a = a2a(jnp.concatenate([contrib_a, gw_block], axis=1))
    contrib_b = (_t_dot(grad_gate, gate_mat[half:]) + _t_dot(grad_up, up_mat[half:])).astype(
        jnp.bfloat16
    )
    back_b = a2a(contrib_b)

    sum_a = jnp.dot(sel_t.T, back_a[:, :half], preferred_element_type=jnp.float32)
    sum_b = jnp.dot(sel_t.T, back_b, preferred_element_type=jnp.float32)
    grad_tokens = jnp.concatenate([sum_a, sum_b], axis=1).astype(jnp.bfloat16)
    gw_back = jnp.dot(sel_a.T, back_a[:, half:], preferred_element_type=jnp.float32)
    grad_combine = gw_back[:, 0].astype(jnp.bfloat16).reshape(token_rows, top_count)
    return (grad_tokens, grad_combine)


def solution(mesh):
    placed = (
        P(("group", "local"), None),
        P(("group", "local"), None),
        P(("group", "local"), None),
        P(("group", "local"), None),
        P(("group", "local"), None, None),
        P(("group", "local"), None, None),
        P(("group", "local"), None, None),
    )
    return jax.shard_map(
        local,
        mesh=mesh,
        in_specs=placed,
        out_specs=(P(("group", "local"), None), P(("group", "local"), None)),
        check_vma=False,
    )
```

```python
import jax
import jax.numpy as jnp
from jax import lax
from jax.sharding import PartitionSpec as P


def _t_dot(a, b):
    return lax.dot_general(a, b, (((1,), (1,)), ((), ())), preferred_element_type=jnp.float32)


def local(tokens, grad_out, expert_ids, combine, gate_weight, up_weight, down_weight):
    token_rows, model_width = tokens.shape
    top_count = expert_ids.shape[1]
    group_count = lax.axis_size("group")
    local_count = lax.axis_size("local")
    expert_count = group_count * local_count
    mean_pair = token_rows * top_count // expert_count
    pair_cap = mean_pair + (mean_pair + 1) // 2
    slot_cap = pair_cap
    gate_mat = gate_weight[0]
    up_mat = up_weight[0]
    down_mat = down_weight[0]
    ff = gate_mat.shape[1]
    assign_count = token_rows * top_count
    lane = 128
    targets = expert_ids.reshape(assign_count)
    one_hot = (targets[:, None] == jnp.arange(expert_count, dtype=jnp.int32)[None, :]).astype(
        jnp.int32
    )
    rank_in = jnp.sum((jnp.cumsum(one_hot, axis=0) - 1) * one_hot, axis=1)
    slot_of = targets * slot_cap + rank_in
    slot_total = expert_count * slot_cap
    sel = slot_of[None, :] == jnp.arange(slot_total, dtype=jnp.int32)[:, None]
    sel_a = sel.astype(jnp.bfloat16)
    sel_t = jnp.any(sel.reshape(slot_total, token_rows, top_count), axis=2).astype(jnp.bfloat16)

    send_x = jnp.dot(sel_t, tokens, preferred_element_type=jnp.bfloat16)
    p_block = jnp.zeros((assign_count, lane), jnp.bfloat16).at[:, 0].set(combine.reshape(assign_count))
    dy_rep = jnp.broadcast_to(grad_out[:, None, :], (token_rows, top_count, model_width)).reshape(
        assign_count, model_width
    )
    send_dyp = jnp.dot(
        sel_a, jnp.concatenate([dy_rep, p_block], axis=1), preferred_element_type=jnp.bfloat16
    )

    def a2a(v):
        width = v.shape[-1]
        v = v.reshape(expert_count, slot_cap * width // lane, lane)
        v = lax.all_to_all(v, ("group", "local"), split_axis=0, concat_axis=0, tiled=True)
        return v.reshape(slot_total, width)

    rows_x = a2a(send_x)
    gate_pre = jnp.dot(rows_x, gate_mat, preferred_element_type=jnp.float32)
    up_pre = jnp.dot(rows_x, up_mat, preferred_element_type=jnp.float32)
    sigmoid_gate = jax.nn.sigmoid(gate_pre)
    active = gate_pre * sigmoid_gate
    hidden = (active * up_pre).astype(jnp.bfloat16)
    output = jnp.dot(hidden, down_mat, preferred_element_type=jnp.float32)
    gate_factor = up_pre * sigmoid_gate * (1.0 + gate_pre * (1.0 - sigmoid_gate))
    gate_factor, active, output = lax.optimization_barrier((gate_factor, active, output))

    rows_dyp = a2a(send_dyp)
    rows_dy = rows_dyp[:, :model_width]
    rows_p = rows_dyp[:, model_width]
    back_hidden = _t_dot(rows_dy, down_mat)
    back_hidden = back_hidden * rows_p.astype(jnp.float32)[:, None]
    grad_gate = (back_hidden * gate_factor).astype(jnp.bfloat16)
    grad_up = (back_hidden * active).astype(jnp.bfloat16)

    half = model_width // 2
    contrib_a = (_t_dot(grad_gate, gate_mat[:half]) + _t_dot(grad_up, up_mat[:half])).astype(
        jnp.bfloat16
    )
    back_a = a2a(contrib_a)
    contrib_b = (_t_dot(grad_gate, gate_mat[half:]) + _t_dot(grad_up, up_mat[half:])).astype(
        jnp.bfloat16
    )
    grad_weight = jnp.sum(rows_dy.astype(jnp.float32) * output, axis=1).astype(jnp.bfloat16)
    gw_block = jnp.zeros((slot_total, lane), jnp.bfloat16).at[:, 0].set(grad_weight)
    back_b = a2a(jnp.concatenate([contrib_b, gw_block], axis=1))

    sum_a = jnp.dot(sel_t.T, back_a, preferred_element_type=jnp.float32)
    sum_b = jnp.dot(sel_t.T, back_b[:, : model_width - half], preferred_element_type=jnp.float32)
    grad_tokens = jnp.concatenate([sum_a, sum_b], axis=1).astype(jnp.bfloat16)
    gw_back = jnp.dot(sel_a.T, back_b[:, model_width - half :], preferred_element_type=jnp.float32)
    grad_combine = gw_back[:, 0].astype(jnp.bfloat16).reshape(token_rows, top_count)
    return (grad_tokens, grad_combine)


def solution(mesh):
    placed = (
        P(("group", "local"), None),
        P(("group", "local"), None),
        P(("group", "local"), None),
        P(("group", "local"), None),
        P(("group", "local"), None, None),
        P(("group", "local"), None, None),
        P(("group", "local"), None, None),
    )
    return jax.shard_map(
        local,
        mesh=mesh,
        in_specs=placed,
        out_specs=(P(("group", "local"), None), P(("group", "local"), None)),
        check_vma=False,
    )
```

```python
import jax
import jax.numpy as jnp
from jax import lax
from jax.sharding import PartitionSpec as P


def _t_dot(a, b):
    return lax.dot_general(a, b, (((1,), (1,)), ((), ())), preferred_element_type=jnp.float32)


def local(tokens, grad_out, expert_ids, combine, gate_weight, up_weight, down_weight):
    token_rows, model_width = tokens.shape
    top_count = expert_ids.shape[1]
    group_count = lax.axis_size("group")
    local_count = lax.axis_size("local")
    expert_count = group_count * local_count
    mean_pair = token_rows * top_count // expert_count
    pair_cap = mean_pair + (mean_pair + 1) // 2
    slot_cap = pair_cap
    gate_mat = gate_weight[0]
    up_mat = up_weight[0]
    down_mat = down_weight[0]
    ff = gate_mat.shape[1]
    assign_count = token_rows * top_count
    lane = 128
    targets = expert_ids.reshape(assign_count)
    one_hot = (targets[:, None] == jnp.arange(expert_count, dtype=jnp.int32)[None, :]).astype(
        jnp.int32
    )
    rank_in = jnp.sum((jnp.cumsum(one_hot, axis=0) - 1) * one_hot, axis=1)
    slot_of = targets * slot_cap + rank_in
    slot_total = expert_count * slot_cap
    sel = slot_of[None, :] == jnp.arange(slot_total, dtype=jnp.int32)[:, None]
    sel_a = sel.astype(jnp.bfloat16)
    sel_t = jnp.any(sel.reshape(slot_total, token_rows, top_count), axis=2).astype(jnp.bfloat16)

    send_x = jnp.dot(sel_t, tokens, preferred_element_type=jnp.bfloat16)
    cols = jnp.arange(lane, dtype=jnp.int32)[None, :]
    info = jnp.zeros((token_rows, lane), jnp.bfloat16)
    for k in range(top_count):
        info = jnp.where(cols == k, combine[:, k : k + 1], info)
        info = jnp.where(cols == top_count + k, expert_ids[:, k : k + 1].astype(jnp.bfloat16), info)
    send_dyp = jnp.dot(
        sel_t, jnp.concatenate([grad_out, info], axis=1), preferred_element_type=jnp.bfloat16
    )

    def a2a(v):
        width = v.shape[-1]
        v = v.reshape(expert_count, slot_cap * width // lane, lane)
        v = lax.all_to_all(v, ("group", "local"), split_axis=0, concat_axis=0, tiled=True)
        return v.reshape(slot_total, width)

    rows_x = a2a(send_x)
    gate_pre = jnp.dot(rows_x, gate_mat, preferred_element_type=jnp.float32)
    up_pre = jnp.dot(rows_x, up_mat, preferred_element_type=jnp.float32)
    sigmoid_gate = jax.nn.sigmoid(gate_pre)
    active = gate_pre * sigmoid_gate
    hidden = (active * up_pre).astype(jnp.bfloat16)
    output = jnp.dot(hidden, down_mat, preferred_element_type=jnp.float32)
    gate_factor = up_pre * sigmoid_gate * (1.0 + gate_pre * (1.0 - sigmoid_gate))
    gate_factor, active, output = lax.optimization_barrier((gate_factor, active, output))

    rows_dyp = a2a(send_dyp)
    rows_dy = rows_dyp[:, :model_width]
    e_me = (lax.axis_index("group") * local_count + lax.axis_index("local")).astype(jnp.float32)
    info_rows = rows_dyp[:, model_width : model_width + 2 * top_count].astype(jnp.float32)
    rows_p = jnp.sum(
        jnp.where(info_rows[:, top_count:] == e_me, info_rows[:, :top_count], 0.0), axis=1
    )
    back_hidden = _t_dot(rows_dy, down_mat)
    back_hidden = back_hidden * rows_p[:, None]
    grad_gate = (back_hidden * gate_factor).astype(jnp.bfloat16)
    grad_up = (back_hidden * active).astype(jnp.bfloat16)

    half = model_width // 2
    contrib_a = (_t_dot(grad_gate, gate_mat[:half]) + _t_dot(grad_up, up_mat[:half])).astype(
        jnp.bfloat16
    )
    back_a = a2a(contrib_a)
    contrib_b = (_t_dot(grad_gate, gate_mat[half:]) + _t_dot(grad_up, up_mat[half:])).astype(
        jnp.bfloat16
    )
    grad_weight = jnp.sum(rows_dy.astype(jnp.float32) * output, axis=1).astype(jnp.bfloat16)
    gw_block = jnp.zeros((slot_total, lane), jnp.bfloat16).at[:, 0].set(grad_weight)
    back_b = a2a(jnp.concatenate([contrib_b, gw_block], axis=1))

    sum_a = jnp.dot(sel_t.T, back_a, preferred_element_type=jnp.float32)
    sum_b = jnp.dot(sel_t.T, back_b[:, : model_width - half], preferred_element_type=jnp.float32)
    grad_tokens = jnp.concatenate([sum_a, sum_b], axis=1).astype(jnp.bfloat16)
    gw_back = jnp.dot(sel_a.T, back_b[:, model_width - half :], preferred_element_type=jnp.float32)
    grad_combine = gw_back[:, 0].astype(jnp.bfloat16).reshape(token_rows, top_count)
    return (grad_tokens, grad_combine)


def solution(mesh):
    placed = (
        P(("group", "local"), None),
        P(("group", "local"), None),
        P(("group", "local"), None),
        P(("group", "local"), None),
        P(("group", "local"), None, None),
        P(("group", "local"), None, None),
        P(("group", "local"), None, None),
    )
    return jax.shard_map(
        local,
        mesh=mesh,
        in_specs=placed,
        out_specs=(P(("group", "local"), None), P(("group", "local"), None)),
        check_vma=False,
    )
```

```python
import jax
import jax.numpy as jnp
from jax import lax
from jax.experimental.layout import Layout, with_layout_constraint
from jax.sharding import PartitionSpec as P


def _t_dot(a, b):
    return lax.dot_general(a, b, (((1,), (1,)), ((), ())), preferred_element_type=jnp.float32)


def local(tokens, grad_out, expert_ids, combine, gate_weight, up_weight, down_weight):
    token_rows, model_width = tokens.shape
    top_count = expert_ids.shape[1]
    group_count = lax.axis_size("group")
    local_count = lax.axis_size("local")
    expert_count = group_count * local_count
    mean_pair = token_rows * top_count // expert_count
    pair_cap = mean_pair + (mean_pair + 1) // 2
    slot_cap = pair_cap
    gate_mat = gate_weight[0]
    up_mat = up_weight[0]
    down_mat = down_weight[0]
    ff = gate_mat.shape[1]
    assign_count = token_rows * top_count
    lane = 128
    targets = expert_ids.reshape(assign_count)
    one_hot = (targets[:, None] == jnp.arange(expert_count, dtype=jnp.int32)[None, :]).astype(
        jnp.int32
    )
    rank_in = jnp.sum((jnp.cumsum(one_hot, axis=0) - 1) * one_hot, axis=1)
    slot_of = targets * slot_cap + rank_in
    slot_total = expert_count * slot_cap
    sel = slot_of[None, :] == jnp.arange(slot_total, dtype=jnp.int32)[:, None]
    sel_a = sel.astype(jnp.bfloat16)
    sel_t = jnp.any(sel.reshape(slot_total, token_rows, top_count), axis=2).astype(jnp.bfloat16)

    send_x = jnp.dot(sel_t, tokens, preferred_element_type=jnp.bfloat16)
    cols = jnp.arange(lane, dtype=jnp.int32)[None, :]
    info = jnp.zeros((token_rows, lane), jnp.bfloat16)
    for k in range(top_count):
        info = jnp.where(cols == k, combine[:, k : k + 1], info)
        info = jnp.where(cols == top_count + k, expert_ids[:, k : k + 1].astype(jnp.bfloat16), info)
    send_dyp = jnp.dot(
        sel_t, jnp.concatenate([grad_out, info], axis=1), preferred_element_type=jnp.bfloat16
    )

    def a2a(v):
        width = v.shape[-1]
        v = v.reshape(expert_count, slot_cap * width // lane, lane)
        v = lax.all_to_all(v, ("group", "local"), split_axis=0, concat_axis=0, tiled=True)
        return v.reshape(slot_total, width)

    row_major = Layout(major_to_minor=(0, 1))
    gate_t, up_t, down_t = (
        with_layout_constraint(w.T, row_major) for w in (gate_mat, up_mat, down_mat)
    )
    rows_x = a2a(send_x)
    gate_pre = jnp.dot(rows_x, gate_mat, preferred_element_type=jnp.float32)
    up_pre = jnp.dot(rows_x, up_mat, preferred_element_type=jnp.float32)
    sigmoid_gate = jax.nn.sigmoid(gate_pre)
    active = gate_pre * sigmoid_gate
    hidden = (active * up_pre).astype(jnp.bfloat16)
    gate_factor = up_pre * sigmoid_gate * (1.0 + gate_pre * (1.0 - sigmoid_gate))
    gate_factor, active, hidden = lax.optimization_barrier((gate_factor, active, hidden))

    rows_dyp = a2a(send_dyp)
    rows_dy = rows_dyp[:, :model_width]
    e_me = (lax.axis_index("group") * local_count + lax.axis_index("local")).astype(jnp.float32)
    info_rows = rows_dyp[:, model_width : model_width + 2 * top_count].astype(jnp.float32)
    rows_p = jnp.sum(
        jnp.where(info_rows[:, top_count:] == e_me, info_rows[:, :top_count], 0.0), axis=1
    )
    back_raw = jnp.dot(rows_dy, down_t, preferred_element_type=jnp.float32)
    grad_weight = jnp.sum(hidden.astype(jnp.float32) * back_raw, axis=1).astype(jnp.bfloat16)
    back_hidden = back_raw * rows_p[:, None]
    grad_gate = (back_hidden * gate_factor).astype(jnp.bfloat16)
    grad_up = (back_hidden * active).astype(jnp.bfloat16)

    half = model_width // 2
    contrib_a = (
        jnp.dot(grad_gate, gate_t[:, :half], preferred_element_type=jnp.float32)
        + jnp.dot(grad_up, up_t[:, :half], preferred_element_type=jnp.float32)
    ).astype(jnp.bfloat16)
    back_a = a2a(contrib_a)
    contrib_b = (
        jnp.dot(grad_gate, gate_t[:, half:], preferred_element_type=jnp.float32)
        + jnp.dot(grad_up, up_t[:, half:], preferred_element_type=jnp.float32)
    ).astype(jnp.bfloat16)
    gw_block = jnp.zeros((slot_total, lane), jnp.bfloat16).at[:, 0].set(grad_weight)
    back_b = a2a(jnp.concatenate([contrib_b, gw_block], axis=1))

    sum_a = jnp.dot(sel_t.T, back_a, preferred_element_type=jnp.float32)
    sum_b = jnp.dot(sel_t.T, back_b[:, : model_width - half], preferred_element_type=jnp.float32)
    grad_tokens = jnp.concatenate([sum_a, sum_b], axis=1).astype(jnp.bfloat16)
    gw_back = jnp.dot(sel_a.T, back_b[:, model_width - half :], preferred_element_type=jnp.float32)
    grad_combine = gw_back[:, 0].astype(jnp.bfloat16).reshape(token_rows, top_count)
    return (grad_tokens, grad_combine)


def solution(mesh):
    placed = (
        P(("group", "local"), None),
        P(("group", "local"), None),
        P(("group", "local"), None),
        P(("group", "local"), None),
        P(("group", "local"), None, None),
        P(("group", "local"), None, None),
        P(("group", "local"), None, None),
    )
    return jax.shard_map(
        local,
        mesh=mesh,
        in_specs=placed,
        out_specs=(P(("group", "local"), None), P(("group", "local"), None)),
        check_vma=False,
    )
```

```python
import jax
import jax.numpy as jnp
from jax import lax
from jax.sharding import PartitionSpec as P


def _t_dot(a, b):
    return lax.dot_general(a, b, (((1,), (1,)), ((), ())), preferred_element_type=jnp.float32)


def local(tokens, grad_out, expert_ids, combine, gate_weight, up_weight, down_weight):
    token_rows, model_width = tokens.shape
    top_count = expert_ids.shape[1]
    group_count = lax.axis_size("group")
    local_count = lax.axis_size("local")
    expert_count = group_count * local_count
    mean_pair = token_rows * top_count // expert_count
    pair_cap = mean_pair + (mean_pair + 1) // 2
    slot_cap = pair_cap
    gate_mat = gate_weight[0]
    up_mat = up_weight[0]
    down_mat = down_weight[0]
    ff = gate_mat.shape[1]
    assign_count = token_rows * top_count
    lane = 128
    targets = expert_ids.reshape(assign_count)
    one_hot = (targets[:, None] == jnp.arange(expert_count, dtype=jnp.int32)[None, :]).astype(
        jnp.int32
    )
    rank_in = jnp.sum((jnp.cumsum(one_hot, axis=0) - 1) * one_hot, axis=1)
    slot_of = targets * slot_cap + rank_in
    slot_total = expert_count * slot_cap
    sel = slot_of[None, :] == jnp.arange(slot_total, dtype=jnp.int32)[:, None]
    sel_a = sel.astype(jnp.bfloat16)
    sel_t = jnp.any(sel.reshape(slot_total, token_rows, top_count), axis=2).astype(jnp.bfloat16)

    send_x = jnp.dot(sel_t, tokens, preferred_element_type=jnp.bfloat16)
    cols = jnp.arange(lane, dtype=jnp.int32)[None, :]
    info = jnp.zeros((token_rows, lane), jnp.bfloat16)
    for k in range(top_count):
        info = jnp.where(cols == k, combine[:, k : k + 1], info)
        info = jnp.where(cols == top_count + k, expert_ids[:, k : k + 1].astype(jnp.bfloat16), info)
    send_dyp = jnp.dot(
        sel_t, jnp.concatenate([grad_out, info], axis=1), preferred_element_type=jnp.bfloat16
    )

    def a2a(v):
        width = v.shape[-1]
        v = v.reshape(expert_count, slot_cap * width // lane, lane)
        v = lax.all_to_all(v, ("group", "local"), split_axis=0, concat_axis=0, tiled=True)
        return v.reshape(slot_total, width)

    rows_x = a2a(send_x)
    gate_pre = jnp.dot(rows_x, gate_mat, preferred_element_type=jnp.float32)
    up_pre = jnp.dot(rows_x, up_mat, preferred_element_type=jnp.float32)
    sigmoid_gate = jax.nn.sigmoid(gate_pre)
    active = gate_pre * sigmoid_gate
    hidden = (active * up_pre).astype(jnp.bfloat16)
    gate_factor = up_pre * sigmoid_gate * (1.0 + gate_pre * (1.0 - sigmoid_gate))
    gate_factor, active, hidden = lax.optimization_barrier((gate_factor, active, hidden))

    rows_dyp = a2a(send_dyp)
    rows_dy = rows_dyp[:, :model_width]
    e_me = (lax.axis_index("group") * local_count + lax.axis_index("local")).astype(jnp.float32)
    info_rows = rows_dyp[:, model_width : model_width + 2 * top_count].astype(jnp.float32)
    rows_p = jnp.sum(
        jnp.where(info_rows[:, top_count:] == e_me, info_rows[:, :top_count], 0.0), axis=1
    )
    back_raw = _t_dot(rows_dy, down_mat)
    grad_weight = jnp.sum(hidden.astype(jnp.float32) * back_raw, axis=1).astype(jnp.bfloat16)
    back_hidden = back_raw * rows_p[:, None]
    grad_gate = (back_hidden * gate_factor).astype(jnp.bfloat16)
    grad_up = (back_hidden * active).astype(jnp.bfloat16)

    half = model_width * 3 // 7 // (lane // 2) * (lane // 2)
    contrib_a = (_t_dot(grad_gate, gate_mat[:half]) + _t_dot(grad_up, up_mat[:half])).astype(
        jnp.bfloat16
    )
    gw_block = jnp.zeros((slot_total, lane), jnp.bfloat16).at[:, 0].set(grad_weight)
    back_a = a2a(jnp.concatenate([contrib_a, gw_block], axis=1))
    contrib_b = (_t_dot(grad_gate, gate_mat[half:]) + _t_dot(grad_up, up_mat[half:])).astype(
        jnp.bfloat16
    )
    back_b = a2a(contrib_b)

    sum_a = jnp.dot(sel_t.T, back_a[:, :half], preferred_element_type=jnp.float32)
    sum_b = jnp.dot(sel_t.T, back_b, preferred_element_type=jnp.float32)
    grad_tokens = jnp.concatenate([sum_a, sum_b], axis=1).astype(jnp.bfloat16)
    gw_back = jnp.dot(sel_a.T, back_a[:, half:], preferred_element_type=jnp.float32)
    grad_combine = gw_back[:, 0].astype(jnp.bfloat16).reshape(token_rows, top_count)
    return (grad_tokens, grad_combine)


def solution(mesh):
    placed = (
        P(("group", "local"), None),
        P(("group", "local"), None),
        P(("group", "local"), None),
        P(("group", "local"), None),
        P(("group", "local"), None, None),
        P(("group", "local"), None, None),
        P(("group", "local"), None, None),
    )
    return jax.shard_map(
        local,
        mesh=mesh,
        in_specs=placed,
        out_specs=(P(("group", "local"), None), P(("group", "local"), None)),
        check_vma=False,
    )
```

```python
import jax
import jax.numpy as jnp
from jax import lax
from jax.sharding import PartitionSpec as P


def _t_dot(a, b):
    return lax.dot_general(a, b, (((1,), (1,)), ((), ())), preferred_element_type=jnp.float32)


def local(tokens, grad_out, expert_ids, combine, gate_weight, up_weight, down_weight):
    token_rows, model_width = tokens.shape
    top_count = expert_ids.shape[1]
    group_count = lax.axis_size("group")
    local_count = lax.axis_size("local")
    expert_count = group_count * local_count
    mean_pair = token_rows * top_count // expert_count
    pair_cap = mean_pair + (mean_pair + 1) // 2
    slot_cap = pair_cap
    gate_mat = gate_weight[0]
    up_mat = up_weight[0]
    down_mat = down_weight[0]
    ff = gate_mat.shape[1]
    assign_count = token_rows * top_count
    lane = 128
    targets = expert_ids.reshape(assign_count)
    one_hot = (targets[:, None] == jnp.arange(expert_count, dtype=jnp.int32)[None, :]).astype(
        jnp.int32
    )
    rank_in = jnp.sum((jnp.cumsum(one_hot, axis=0) - 1) * one_hot, axis=1)
    slot_of = targets * slot_cap + rank_in
    slot_total = expert_count * slot_cap
    sel = slot_of[None, :] == jnp.arange(slot_total, dtype=jnp.int32)[:, None]
    sel_a = sel.astype(jnp.bfloat16)
    sel_t = jnp.any(sel.reshape(slot_total, token_rows, top_count), axis=2).astype(jnp.bfloat16)

    send_x = jnp.dot(sel_t, tokens, preferred_element_type=jnp.bfloat16)
    cols = jnp.arange(lane, dtype=jnp.int32)[None, :]
    info = jnp.zeros((token_rows, lane), jnp.bfloat16)
    for k in range(top_count):
        info = jnp.where(cols == k, combine[:, k : k + 1], info)
        info = jnp.where(cols == top_count + k, expert_ids[:, k : k + 1].astype(jnp.bfloat16), info)
    send_dyp = jnp.dot(
        sel_t, jnp.concatenate([grad_out, info], axis=1), preferred_element_type=jnp.bfloat16
    )

    def a2a(v):
        width = v.shape[-1]
        v = v.reshape(expert_count, slot_cap * width // lane, lane)
        v = lax.all_to_all(v, ("group", "local"), split_axis=0, concat_axis=0, tiled=True)
        return v.reshape(slot_total, width)

    rows_x = a2a(send_x)
    gate_pre = jnp.dot(rows_x, gate_mat, preferred_element_type=jnp.float32)
    up_pre = jnp.dot(rows_x, up_mat, preferred_element_type=jnp.float32)
    sigmoid_gate = jax.nn.sigmoid(gate_pre)
    active = gate_pre * sigmoid_gate
    hidden = (active * up_pre).astype(jnp.bfloat16)
    gate_factor = up_pre * sigmoid_gate * (1.0 + gate_pre * (1.0 - sigmoid_gate))
    gate_factor, active, hidden = lax.optimization_barrier((gate_factor, active, hidden))

    rows_dyp = a2a(send_dyp)
    rows_dy = rows_dyp[:, :model_width]
    e_me = (lax.axis_index("group") * local_count + lax.axis_index("local")).astype(jnp.float32)
    info_rows = rows_dyp[:, model_width : model_width + 2 * top_count].astype(jnp.float32)
    rows_p = jnp.sum(
        jnp.where(info_rows[:, top_count:] == e_me, info_rows[:, :top_count], 0.0), axis=1
    )
    back_raw = _t_dot(rows_dy, down_mat)
    grad_weight = jnp.sum(hidden.astype(jnp.float32) * back_raw, axis=1).astype(jnp.bfloat16)
    back_hidden = back_raw * rows_p[:, None]
    grad_gate = (back_hidden * gate_factor).astype(jnp.bfloat16)
    grad_up = (back_hidden * active).astype(jnp.bfloat16)

    half = model_width * 2 // 7 // (lane // 2) * (lane // 2)
    contrib_a = (_t_dot(grad_gate, gate_mat[:half]) + _t_dot(grad_up, up_mat[:half])).astype(
        jnp.bfloat16
    )
    gw_block = jnp.zeros((slot_total, lane), jnp.bfloat16).at[:, 0].set(grad_weight)
    back_a = a2a(jnp.concatenate([contrib_a, gw_block], axis=1))
    contrib_b = (_t_dot(grad_gate, gate_mat[half:]) + _t_dot(grad_up, up_mat[half:])).astype(
        jnp.bfloat16
    )
    back_b = a2a(contrib_b)

    sum_a = jnp.dot(sel_t.T, back_a[:, :half], preferred_element_type=jnp.float32)
    sum_b = jnp.dot(sel_t.T, back_b, preferred_element_type=jnp.float32)
    grad_tokens = jnp.concatenate([sum_a, sum_b], axis=1).astype(jnp.bfloat16)
    gw_back = jnp.dot(sel_a.T, back_a[:, half:], preferred_element_type=jnp.float32)
    grad_combine = gw_back[:, 0].astype(jnp.bfloat16).reshape(token_rows, top_count)
    return (grad_tokens, grad_combine)


def solution(mesh):
    placed = (
        P(("group", "local"), None),
        P(("group", "local"), None),
        P(("group", "local"), None),
        P(("group", "local"), None),
        P(("group", "local"), None, None),
        P(("group", "local"), None, None),
        P(("group", "local"), None, None),
    )
    return jax.shard_map(
        local,
        mesh=mesh,
        in_specs=placed,
        out_specs=(P(("group", "local"), None), P(("group", "local"), None)),
        check_vma=False,
    )
```

```python
import jax
import jax.numpy as jnp
from jax import lax
from jax.sharding import PartitionSpec as P


def _t_dot(a, b):
    return lax.dot_general(a, b, (((1,), (1,)), ((), ())), preferred_element_type=jnp.float32)


def local(tokens, grad_out, expert_ids, combine, gate_weight, up_weight, down_weight):
    token_rows, model_width = tokens.shape
    top_count = expert_ids.shape[1]
    group_count = lax.axis_size("group")
    local_count = lax.axis_size("local")
    expert_count = group_count * local_count
    mean_pair = token_rows * top_count // expert_count
    pair_cap = mean_pair + (mean_pair + 1) // 2
    slot_cap = pair_cap
    gate_mat = gate_weight[0]
    up_mat = up_weight[0]
    down_mat = down_weight[0]
    ff = gate_mat.shape[1]
    assign_count = token_rows * top_count
    lane = 128
    targets = expert_ids.reshape(assign_count)
    one_hot = (targets[:, None] == jnp.arange(expert_count, dtype=jnp.int32)[None, :]).astype(
        jnp.int32
    )
    rank_in = jnp.sum((jnp.cumsum(one_hot, axis=0) - 1) * one_hot, axis=1)
    slot_of = targets * slot_cap + rank_in
    slot_total = expert_count * slot_cap
    sel = slot_of[None, :] == jnp.arange(slot_total, dtype=jnp.int32)[:, None]
    sel_a = sel.astype(jnp.bfloat16)
    sel_t = jnp.any(sel.reshape(slot_total, token_rows, top_count), axis=2).astype(jnp.bfloat16)

    cols = jnp.arange(lane, dtype=jnp.int32)[None, :]
    info = jnp.zeros((token_rows, lane), jnp.bfloat16)
    for k in range(top_count):
        info = jnp.where(cols == k, combine[:, k : k + 1], info)
        info = jnp.where(cols == top_count + k, expert_ids[:, k : k + 1].astype(jnp.bfloat16), info)
    send_x = jnp.dot(
        sel_t, jnp.concatenate([tokens, info], axis=1), preferred_element_type=jnp.bfloat16
    )
    send_dy = jnp.dot(sel_t, grad_out, preferred_element_type=jnp.bfloat16)

    def a2a(v):
        width = v.shape[-1]
        v = v.reshape(expert_count, slot_cap * width // lane, lane)
        v = lax.all_to_all(v, ("group", "local"), split_axis=0, concat_axis=0, tiled=True)
        return v.reshape(slot_total, width)

    info_width = model_width + lane
    rows_xi = lax.all_to_all(
        send_x.reshape(expert_count, slot_cap * info_width // lane, lane),
        ("group", "local"), split_axis=0, concat_axis=0, tiled=True,
    )
    send_dy = send_dy.reshape(expert_count, slot_cap * model_width // lane, lane)
    rows_xi, send_dy = lax.optimization_barrier((rows_xi, send_dy))
    rows_xi = rows_xi.reshape(slot_total, info_width)
    rows_x = rows_xi[:, :model_width]
    e_me = (lax.axis_index("group") * local_count + lax.axis_index("local")).astype(jnp.float32)
    info_rows = rows_xi[:, model_width : model_width + 2 * top_count].astype(jnp.float32)
    rows_p = jnp.sum(
        jnp.where(info_rows[:, top_count:] == e_me, info_rows[:, :top_count], 0.0), axis=1
    )
    gate_pre = jnp.dot(rows_x, gate_mat, preferred_element_type=jnp.float32)
    up_pre = jnp.dot(rows_x, up_mat, preferred_element_type=jnp.float32)
    sigmoid_gate = jax.nn.sigmoid(gate_pre)
    active = gate_pre * sigmoid_gate
    hidden = (active * up_pre).astype(jnp.bfloat16)
    gate_factor = up_pre * sigmoid_gate * (1.0 + gate_pre * (1.0 - sigmoid_gate))
    gate_factor, active, hidden, rows_p = lax.optimization_barrier(
        (gate_factor, active, hidden, rows_p)
    )

    rows_dy = lax.all_to_all(send_dy, ("group", "local"), split_axis=0, concat_axis=0, tiled=True)
    rows_dy = rows_dy.reshape(slot_total, model_width)
    back_raw = _t_dot(rows_dy, down_mat)
    grad_weight = jnp.sum(hidden.astype(jnp.float32) * back_raw, axis=1).astype(jnp.bfloat16)
    back_hidden = back_raw * rows_p[:, None]
    grad_gate = (back_hidden * gate_factor).astype(jnp.bfloat16)
    grad_up = (back_hidden * active).astype(jnp.bfloat16)

    half = model_width * 2 // 7 // (lane // 2) * (lane // 2)
    contrib_a = (_t_dot(grad_gate, gate_mat[:half]) + _t_dot(grad_up, up_mat[:half])).astype(
        jnp.bfloat16
    )
    gw_block = jnp.zeros((slot_total, lane), jnp.bfloat16).at[:, 0].set(grad_weight)
    back_a = a2a(jnp.concatenate([contrib_a, gw_block], axis=1))
    contrib_b = (_t_dot(grad_gate, gate_mat[half:]) + _t_dot(grad_up, up_mat[half:])).astype(
        jnp.bfloat16
    )
    back_b = a2a(contrib_b)

    sum_a = jnp.dot(sel_t.T, back_a[:, :half], preferred_element_type=jnp.float32)
    sum_b = jnp.dot(sel_t.T, back_b, preferred_element_type=jnp.float32)
    grad_tokens = jnp.concatenate([sum_a, sum_b], axis=1).astype(jnp.bfloat16)
    gw_back = jnp.dot(sel_a.T, back_a[:, half:], preferred_element_type=jnp.float32)
    grad_combine = gw_back[:, 0].astype(jnp.bfloat16).reshape(token_rows, top_count)
    return (grad_tokens, grad_combine)


def solution(mesh):
    placed = (
        P(("group", "local"), None),
        P(("group", "local"), None),
        P(("group", "local"), None),
        P(("group", "local"), None),
        P(("group", "local"), None, None),
        P(("group", "local"), None, None),
        P(("group", "local"), None, None),
    )
    return jax.shard_map(
        local,
        mesh=mesh,
        in_specs=placed,
        out_specs=(P(("group", "local"), None), P(("group", "local"), None)),
        check_vma=False,
    )
```

```python
import jax
import jax.numpy as jnp
from jax import lax
from jax.sharding import PartitionSpec as P


def _t_dot(a, b):
    return lax.dot_general(a, b, (((1,), (1,)), ((), ())), preferred_element_type=jnp.float32)


def local(tokens, grad_out, expert_ids, combine, gate_weight, up_weight, down_weight):
    token_rows, model_width = tokens.shape
    top_count = expert_ids.shape[1]
    group_count = lax.axis_size("group")
    local_count = lax.axis_size("local")
    expert_count = group_count * local_count
    mean_pair = token_rows * top_count // expert_count
    pair_cap = mean_pair + (mean_pair + 1) // 2
    slot_cap = pair_cap
    gate_mat = gate_weight[0]
    up_mat = up_weight[0]
    down_mat = down_weight[0]
    ff = gate_mat.shape[1]
    assign_count = token_rows * top_count
    lane = 128
    targets = expert_ids.reshape(assign_count)
    one_hot = (targets[:, None] == jnp.arange(expert_count, dtype=jnp.int32)[None, :]).astype(
        jnp.int32
    )
    rank_in = jnp.sum((jnp.cumsum(one_hot, axis=0) - 1) * one_hot, axis=1)
    slot_of = targets * slot_cap + rank_in
    slot_total = expert_count * slot_cap
    sel = slot_of[None, :] == jnp.arange(slot_total, dtype=jnp.int32)[:, None]
    sel_a = sel.astype(jnp.bfloat16)
    sel_t = jnp.any(sel.reshape(slot_total, token_rows, top_count), axis=2).astype(jnp.bfloat16)

    send_x = jnp.dot(sel_t, tokens, preferred_element_type=jnp.bfloat16)
    cols = jnp.arange(lane, dtype=jnp.int32)[None, :]
    info = jnp.zeros((token_rows, lane), jnp.bfloat16)
    for k in range(top_count):
        info = jnp.where(cols == k, combine[:, k : k + 1], info)
        info = jnp.where(cols == top_count + k, expert_ids[:, k : k + 1].astype(jnp.bfloat16), info)
    send_dyp = jnp.dot(
        sel_t, jnp.concatenate([grad_out, info], axis=1), preferred_element_type=jnp.bfloat16
    )

    def a2a(v):
        width = v.shape[-1]
        v = v.reshape(expert_count, slot_cap * width // lane, lane)
        v = lax.all_to_all(v, ("group", "local"), split_axis=0, concat_axis=0, tiled=True)
        return v.reshape(slot_total, width)

    rows_x = a2a(send_x)
    gate_pre = jnp.dot(rows_x, gate_mat, preferred_element_type=jnp.float32)
    up_pre = jnp.dot(rows_x, up_mat, preferred_element_type=jnp.float32)
    sigmoid_gate = jax.nn.sigmoid(gate_pre)
    active = gate_pre * sigmoid_gate
    hidden = (active * up_pre).astype(jnp.bfloat16)
    gate_factor = up_pre * sigmoid_gate * (1.0 + gate_pre * (1.0 - sigmoid_gate))
    gate_factor, active, hidden = lax.optimization_barrier((gate_factor, active, hidden))

    rows_dyp = a2a(send_dyp)
    rows_dy = rows_dyp[:, :model_width]
    e_me = (lax.axis_index("group") * local_count + lax.axis_index("local")).astype(jnp.float32)
    info_rows = rows_dyp[:, model_width : model_width + 2 * top_count].astype(jnp.float32)
    rows_p = jnp.sum(
        jnp.where(info_rows[:, top_count:] == e_me, info_rows[:, :top_count], 0.0), axis=1
    )
    back_raw = _t_dot(rows_dy, down_mat)
    grad_weight = jnp.sum(hidden.astype(jnp.float32) * back_raw, axis=1).astype(jnp.bfloat16)
    back_hidden = back_raw * rows_p[:, None]
    grad_gate = (back_hidden * gate_factor).astype(jnp.bfloat16)
    grad_up = (back_hidden * active).astype(jnp.bfloat16)

    half = model_width * 2 // 7 // (lane // 2) * (lane // 2)
    contrib_a = (_t_dot(grad_gate, gate_mat[:half]) + _t_dot(grad_up, up_mat[:half])).astype(
        jnp.bfloat16
    )
    back_a = a2a(contrib_a)
    contrib_b = (_t_dot(grad_gate, gate_mat[half:]) + _t_dot(grad_up, up_mat[half:])).astype(
        jnp.bfloat16
    )
    gw_block = jnp.zeros((slot_total, lane), jnp.bfloat16).at[:, 0].set(grad_weight)
    back_b = a2a(jnp.concatenate([contrib_b, gw_block], axis=1))

    sum_a = jnp.dot(sel_t.T, back_a, preferred_element_type=jnp.float32)
    sum_b = jnp.dot(sel_t.T, back_b[:, : model_width - half], preferred_element_type=jnp.float32)
    grad_tokens = jnp.concatenate([sum_a, sum_b], axis=1).astype(jnp.bfloat16)
    gw_back = jnp.dot(sel_a.T, back_b[:, model_width - half :], preferred_element_type=jnp.float32)
    grad_combine = gw_back[:, 0].astype(jnp.bfloat16).reshape(token_rows, top_count)
    return (grad_tokens, grad_combine)


def solution(mesh):
    placed = (
        P(("group", "local"), None),
        P(("group", "local"), None),
        P(("group", "local"), None),
        P(("group", "local"), None),
        P(("group", "local"), None, None),
        P(("group", "local"), None, None),
        P(("group", "local"), None, None),
    )
    return jax.shard_map(
        local,
        mesh=mesh,
        in_specs=placed,
        out_specs=(P(("group", "local"), None), P(("group", "local"), None)),
        check_vma=False,
    )
```
